768 devices in a mesh: tm: 8 (over y), rows: 6 (over z_lo), cols: 16 (over z_hi, x, core).
Axes of the slice: x: 4, y: 8, z: 12 (z_hi: 2, z_lo: 6; z = z_hi * 6 + z_lo), core: 2. Of those that a mesh axis runs over, the one named last changes fastest.
Arguments:
- video: bfloat16 [16, 96, 256, 192], P('tm', 'rows', 'cols'), may hold values from -40 to 40, as said below
- cotangent: bfloat16 [16, 96, 256, 192], P('tm', 'rows', 'cols'), may hold values from -40 to 40, as said below
- weight: bfloat16 [5184, 192], P(('rows', 'cols')), may hold values from -0.078125 to 0.078125
- gain: float32 [192], replicated, may hold values from 0.25 to 1.75
- shift: float32 [192], replicated, may hold values from -3 to 3
- conv_bias: float32 [192], replicated, may hold values from -2 to 2
Outputs:
- output: bfloat16 [16, 96, 256, 192], P('tm', 'rows', 'cols')
- grad_video: bfloat16 [16, 96, 256, 192], P('tm', 'rows', 'cols')
- grad_weight: float32 [5184, 192], P(('rows', 'cols'))
- grad_gain: float32 [192], replicated
- grad_shift: float32 [192], replicated
- grad_conv_bias: float32 [192], replicated
The draws below stay inside these ranges and needn't reach their ends.
Inputs may be any that keep to these rules, and one draw needn't show every extreme that they name: `video`: Real-valued activations; their magnitude varies across frames, rows and columns. `cotangent`: Real-valued gradients; their magnitude varies across frames, rows and columns.
All inputs are finite; a program needn't handle non-finite values.
Results may differ from the reference program's by a relative error of at most 0.0031.
Values may be sent and summed in bfloat16 or wider, within the bound.
No kernel may reach another device: no remote copies, remote signals or barrier semaphores. Data moves between devices by JAX's collectives and lax.ppermute only.
A program may use at most 64 MiB of HBM per device.

```python
import jax
import jax.numpy as jnp
from jax import lax

CH = 192
GROUPS = 32
FRAMES = 16
HEIGHT = 96
WIDTH = 256


def ramp_field():
    frame_pos = jnp.arange(FRAMES, dtype=jnp.float32).reshape(FRAMES, 1, 1, 1) / FRAMES
    row_pos = jnp.arange(HEIGHT, dtype=jnp.float32).reshape(1, HEIGHT, 1, 1) / HEIGHT
    col_pos = jnp.arange(WIDTH, dtype=jnp.float32).reshape(1, 1, WIDTH, 1) / WIDTH
    return jnp.exp(jnp.log(3.0) * (frame_pos + row_pos + col_pos - 1.5))


def frame_levels(key):
    level_key = jax.random.fold_in(key, 97)
    exponent = jax.random.uniform(level_key, (FRAMES,), jnp.float32, -0.6, 0.6)
    return jnp.exp(exponent).reshape(FRAMES, 1, 1, 1)


def field_draw(key):
    shape = (FRAMES, HEIGHT, WIDTH, CH)
    base_key = jax.random.fold_in(key, 5)
    base = jax.random.truncated_normal(base_key, -4.0, 4.0, shape, jnp.float32)
    return (base * ramp_field() * frame_levels(key)).astype(jnp.bfloat16)


def draw_video(key, part):
    return field_draw(jax.random.fold_in(key, 11))


def draw_cotangent(key, part):
    return field_draw(jax.random.fold_in(key, 23))


def level_of(stream_key, extent, cuts, low, top_value):
    level = 1.0
    for axis_at, parts in cuts:
        heights = jax.random.uniform(jax.random.fold_in(jax.random.fold_in(stream_key, 6), axis_at), (parts,), jnp.float32, low / len(cuts), top_value / len(cuts))
        level = level * jnp.repeat(jnp.exp(heights), extent[axis_at] // parts).reshape((-1,) + (1,) * (len(extent) - 1 - axis_at))
    return level


def normal_values(rng, dims, scale, bound, cuts=(), kind=jnp.bfloat16):
    values = scale * jax.random.normal(rng, dims, jnp.float32)
    if cuts:
        values = values * level_of(rng, dims, cuts, -0.22, 0.18)
    return jnp.clip(values, -bound, bound).astype(kind)


def setup_inputs(seed: int = 0) -> dict:
    key_list = jax.random.split(jax.random.key(seed), 7)
    return {
        "video": draw_video(jax.random.fold_in(key_list[6], 71), 0),
        "cotangent": draw_cotangent(jax.random.fold_in(key_list[6], 71), 0),
        "weight": normal_values(key_list[2], (27 * CH, CH), (27 * CH) ** -0.5, 0.078125, ((0, 96),)),
        "gain": jnp.clip(1.0 + 0.15 * jax.random.normal(key_list[3], (CH,), jnp.float32), 0.25, 1.75),
        "shift": normal_values(key_list[4], (CH,), 0.5, 3.0, (), jnp.float32),
        "conv_bias": normal_values(key_list[5], (CH,), 0.3, 2.0, (), jnp.float32),
    }


def per_group(values):
    return jnp.repeat(values.reshape(GROUPS, -1).sum(axis=1), CH // GROUPS)

def reference(video, cotangent, weight, gain, shift, conv_bias):
    video_f = video.astype(jnp.float32)
    count = float(FRAMES * HEIGHT * WIDTH * (CH // GROUPS))
    sums = lax.optimization_barrier(jnp.sum(video_f, axis=(0, 1, 2)))
    squares = lax.optimization_barrier(jnp.sum(video_f * video_f, axis=(0, 1, 2)))
    mean_c = per_group(sums) / count
    variance = per_group(squares) / count - mean_c * mean_c
    rstd_c = lax.rsqrt(variance + 1e-06)
    normed = (video_f - mean_c) * rstd_c
    pre = normed * gain + shift
    hidden = jax.nn.silu(pre).astype(jnp.bfloat16)
    padded = jnp.pad(hidden, ((2, 0), (1, 1), (1, 1), (0, 0))).astype(jnp.float32)
    grad_f = cotangent.astype(jnp.float32)
    grad_pad = jnp.pad(grad_f, ((0, 2), (1, 1), (1, 1), (0, 0)))
    kernel = weight.astype(jnp.float32).reshape(27, CH, CH)
    grad_flat = grad_f.reshape(-1, CH)
    total = jnp.zeros((FRAMES * HEIGHT * WIDTH, CH), jnp.float32) + conv_bias
    back_total = jnp.zeros((FRAMES * HEIGHT * WIDTH, CH), jnp.float32)
    kernel_grads = []
    for tap_t in range(3):
        for tap_r in range(3):
            for tap_c in range(3):
                index = (tap_t * 3 + tap_r) * 3 + tap_c
                window = padded[tap_t:tap_t + FRAMES, tap_r:tap_r + HEIGHT, tap_c:tap_c + WIDTH].reshape(-1, CH)
                total = total + jnp.dot(window, kernel[index])
                kernel_grads.append(jnp.dot(window.T, grad_flat))
                grad_win = grad_pad[2 - tap_t:2 - tap_t + FRAMES, 2 - tap_r:2 - tap_r + HEIGHT, 2 - tap_c:2 - tap_c + WIDTH].reshape(-1, CH)
                back_total = back_total + jnp.dot(grad_win, kernel[index].T)
    output = (video_f + total.reshape(FRAMES, HEIGHT, WIDTH, CH)).astype(jnp.bfloat16)
    grad_weight = jnp.stack(kernel_grads).reshape(27 * CH, CH)
    grad_hidden = lax.optimization_barrier(back_total.astype(jnp.bfloat16)).astype(jnp.float32)
    grad_hidden = grad_hidden.reshape(FRAMES, HEIGHT, WIDTH, CH)
    sigma = jax.nn.sigmoid(pre)
    grad_pre = grad_hidden * sigma * (1.0 + pre * (1.0 - sigma))
    grad_gain = lax.optimization_barrier(jnp.sum(grad_pre * normed, axis=(0, 1, 2)))
    grad_shift = lax.optimization_barrier(jnp.sum(grad_pre, axis=(0, 1, 2)))
    grad_conv_bias = lax.optimization_barrier(jnp.sum(grad_f, axis=(0, 1, 2)))
    term_a = per_group(gain * grad_shift) / count
    term_b = per_group(gain * grad_gain) / count
    grad_video = (grad_f + rstd_c * (grad_pre * gain - term_a - normed * term_b)).astype(jnp.bfloat16)
    return (output, grad_video, grad_weight, grad_gain, grad_shift, grad_conv_bias)
```

```python
import jax
import jax.numpy as jnp
from jax import lax
from jax.sharding import PartitionSpec as P

CH = 192
GROUPS = 32


def padded_2(block, sides, width):
    for axis, dim in sides:
        count = lax.axis_size(axis)
        forward = [(i, i + 1) for i in range(count - 1)]
        backward = [(target, source) for source, target in forward]
        low = lax.ppermute(
            lax.slice_in_dim(block, block.shape[dim] - width, None, axis=dim), axis, forward
        )
        high = lax.ppermute(lax.slice_in_dim(block, 0, width, axis=dim), axis, backward)
        block = jnp.concatenate([low, block, high], axis=dim)
    return block


def xor_sum(x, axis):
    n = lax.axis_size(axis)
    step = 1
    while step < n:
        x = x + lax.ppermute(x, axis, [(i, i ^ step) for i in range(n)])
        step *= 2
    return x


def six_sum(x, axis):
    n = lax.axis_size(axis)
    x = x + lax.ppermute(x, axis, [(i, i ^ 1) for i in range(n)])
    here = lax.axis_index(axis) // 2
    ahead = lax.ppermute(x, axis, [(i, (i + 2) % n) for i in range(n)])
    behind = lax.ppermute(x, axis, [(i, (i + 4) % n) for i in range(n)])
    first = jnp.where(here == 0, x, jnp.where(here == 1, ahead, behind))
    second = jnp.where(here == 1, x, jnp.where(here == 2, ahead, behind))
    third = jnp.where(here == 2, x, jnp.where(here == 0, ahead, behind))
    return (first + second) + third


def all_sum(x):
    return xor_sum(six_sum(xor_sum(x, "cols"), "rows"), "tm")


def halve_scatter(q, axis, dim):
    n = lax.axis_size(axis)
    bits = n.bit_length() - 1
    here = lax.axis_index(axis)
    shape = q.shape
    q = q.reshape(shape[:dim] + (2,) * bits + shape[dim + 1 :])
    for level in range(bits):
        step = 1 << level
        at = dim + bits - 1 - level
        bit = (here // step) % 2
        keep = lax.dynamic_index_in_dim(q, bit, axis=at, keepdims=False)
        send = lax.dynamic_index_in_dim(q, 1 - bit, axis=at, keepdims=False)
        q = keep + lax.ppermute(send, axis, [(i, i ^ step) for i in range(n)])
    return q.reshape(shape[:dim] + (1,) + shape[dim + 1 :])


def per_group(values):
    return jnp.repeat(values.reshape(GROUPS, -1).sum(axis=1), CH // GROUPS)


def to_pairs(field, pair_count, local_rows, local_cols, channels):
    paired = field.reshape(pair_count, 2, local_rows, local_cols, channels)
    return paired.transpose(0, 2, 3, 1, 4).reshape(pair_count, local_rows, local_cols, 2 * channels)


def from_pairs(field, local_rows, local_cols, channels):
    pair_count = field.shape[0]
    split = field.reshape(pair_count, local_rows + 2, local_cols + 2, 2, channels)
    return split.transpose(0, 3, 1, 2, 4).reshape(
        2 * pair_count, local_rows + 2, local_cols + 2, channels
    )


def per_device(video, cotangent, weight, gain, shift, conv_bias):
    local_frames, local_rows, local_cols, channels = video.shape
    pair_count = local_frames // 2
    packed = jnp.concatenate(
        [
            to_pairs(video, pair_count, local_rows, local_cols, channels),
            to_pairs(cotangent, pair_count, local_rows, local_cols, channels),
        ],
        axis=-1,
    )
    framed = padded_2(packed, (("tm", 0), ("rows", 1), ("cols", 2)), 1)
    video_ext = from_pairs(
        framed[: pair_count + 1, :, :, : 2 * channels], local_rows, local_cols, channels
    )
    grad_ext = from_pairs(framed[1:, :, :, 2 * channels :], local_rows, local_cols, channels)
    video_f = video.astype(jnp.float32)
    sums, squares = all_sum(
        jnp.stack([jnp.sum(video_f, axis=(0, 1, 2)), jnp.sum(video_f * video_f, axis=(0, 1, 2))])
    )
    devices_all = lax.axis_size("tm") * lax.axis_size("rows") * lax.axis_size("cols")
    count = float(local_frames * local_rows * local_cols * devices_all * (channels // GROUPS))
    mean_c = per_group(sums) / count
    variance = per_group(squares) / count - mean_c * mean_c
    rstd_c = lax.rsqrt(variance + 1e-06)
    normed_ext = (video_ext.astype(jnp.float32) - mean_c) * rstd_c
    pre_ext = normed_ext * gain + shift
    frame_pos = lax.broadcasted_iota(jnp.int32, (local_frames + 2, 1, 1, 1), 0)
    row_pos = lax.broadcasted_iota(jnp.int32, (1, local_rows + 2, 1, 1), 1)
    col_pos = lax.broadcasted_iota(jnp.int32, (1, 1, local_cols + 2, 1), 2)
    time_index = lax.axis_index("tm")
    row_index = lax.axis_index("rows")
    col_index = lax.axis_index("cols")
    valid = (frame_pos >= 2) | (time_index > 0)
    valid = (
        valid
        & ((row_pos > 0) | (row_index > 0))
        & ((row_pos < local_rows + 1) | (row_index < lax.axis_size("rows") - 1))
    )
    valid = (
        valid
        & ((col_pos > 0) | (col_index > 0))
        & ((col_pos < local_cols + 1) | (col_index < lax.axis_size("cols") - 1))
    )
    padded = jnp.where(valid, jax.nn.silu(pre_ext), 0.0).astype(jnp.bfloat16)
    whole = lax.all_gather(weight, ("rows", "cols"), axis=0, tiled=True)
    cells = local_frames * local_rows * local_cols
    windows = []
    grad_windows = []
    for tap_t in range(3):
        for tap_r in range(3):
            for tap_c in range(3):
                windows.append(
                    padded[
                        tap_t : tap_t + local_frames,
                        tap_r : tap_r + local_rows,
                        tap_c : tap_c + local_cols,
                    ]
                )
                grad_windows.append(
                    grad_ext[
                        2 - tap_t : 2 - tap_t + local_frames,
                        2 - tap_r : 2 - tap_r + local_rows,
                        2 - tap_c : 2 - tap_c + local_cols,
                    ]
                )
    patches = jnp.concatenate(windows, axis=-1).reshape(cells, 27 * channels)
    grad_patches = jnp.concatenate(grad_windows, axis=-1).reshape(cells, 27 * channels)
    conv = jnp.dot(patches, whole, preferred_element_type=jnp.float32) + conv_bias
    output = (video_f + conv.reshape(local_frames, local_rows, local_cols, channels)).astype(
        jnp.bfloat16
    )
    grad_flat = cotangent.reshape(cells, channels)
    kernel_grad = lax.dot_general(
        patches, grad_flat, (((0,), (0,)), ((), ())), preferred_element_type=jnp.float32
    )
    flipped = (
        whole.reshape(27, channels, channels).transpose(0, 2, 1).reshape(27 * channels, channels)
    )
    grad_hidden = jnp.dot(grad_patches, flipped, preferred_element_type=jnp.float32).astype(
        jnp.bfloat16
    )
    grad_hidden = lax.optimization_barrier(grad_hidden).astype(jnp.float32)
    grad_hidden = grad_hidden.reshape(local_frames, local_rows, local_cols, channels)
    normed = normed_ext[2:, 1:-1, 1:-1]
    pre = pre_ext[2:, 1:-1, 1:-1]
    sigma = jax.nn.sigmoid(pre)
    grad_pre = grad_hidden * sigma * (1.0 + pre * (1.0 - sigma))
    grad_f = cotangent.astype(jnp.float32)
    gain_part = jnp.sum(grad_pre * normed, axis=(0, 1, 2))
    shift_part = jnp.sum(grad_pre, axis=(0, 1, 2))
    bias_part = jnp.sum(grad_f, axis=(0, 1, 2))
    grad_gain, grad_shift, grad_conv_bias = all_sum(jnp.stack([gain_part, shift_part, bias_part]))
    row_count = lax.axis_size("rows")
    col_count = lax.axis_size("cols")
    band = kernel_grad.reshape(row_count, col_count, -1, channels)
    band = halve_scatter(band, "cols", 1)
    band = lax.psum_scatter(band, "rows", scatter_dimension=0, tiled=True)
    grad_weight = xor_sum(band.reshape(-1, channels), "tm")
    term_a = per_group(gain * grad_shift) / count
    term_b = per_group(gain * grad_gain) / count
    grad_video = (grad_f + rstd_c * (grad_pre * gain - term_a - normed * term_b)).astype(
        jnp.bfloat16
    )
    return (output, grad_video, grad_weight, grad_gain, grad_shift, grad_conv_bias)


def solution(mesh):
    return jax.shard_map(
        per_device,
        mesh=mesh,
        in_specs=(
            P("tm", "rows", "cols", None),
            P("tm", "rows", "cols", None),
            P(("rows", "cols"), None),
            P(),
            P(),
            P(),
        ),
        out_specs=(
            P("tm", "rows", "cols", None),
            P("tm", "rows", "cols", None),
            P(("rows", "cols"), None),
            P(),
            P(),
            P(),
        ),
        check_vma=False,
    )
```

```python
import jax
import jax.numpy as jnp
from jax import lax
from jax.sharding import PartitionSpec as P

CH = 192
GROUPS = 32


def padded_2(block, sides, width):
    for axis, dim in sides:
        count = lax.axis_size(axis)
        forward = [(i, i + 1) for i in range(count - 1)]
        backward = [(target, source) for source, target in forward]
        low = lax.ppermute(
            lax.slice_in_dim(block, block.shape[dim] - width, None, axis=dim), axis, forward
        )
        high = lax.ppermute(lax.slice_in_dim(block, 0, width, axis=dim), axis, backward)
        block = jnp.concatenate([low, block, high], axis=dim)
    return block


def xor_sum(x, axis):
    n = lax.axis_size(axis)
    step = 1
    while step < n:
        x = x + lax.ppermute(x, axis, [(i, i ^ step) for i in range(n)])
        step *= 2
    return x


def six_sum(x, axis):
    n = lax.axis_size(axis)
    x = x + lax.ppermute(x, axis, [(i, i ^ 1) for i in range(n)])
    here = lax.axis_index(axis) // 2
    ahead = lax.ppermute(x, axis, [(i, (i + 2) % n) for i in range(n)])
    behind = lax.ppermute(x, axis, [(i, (i + 4) % n) for i in range(n)])
    first = jnp.where(here == 0, x, jnp.where(here == 1, ahead, behind))
    second = jnp.where(here == 1, x, jnp.where(here == 2, ahead, behind))
    third = jnp.where(here == 2, x, jnp.where(here == 0, ahead, behind))
    return (first + second) + third


def all_sum(x):
    return xor_sum(six_sum(xor_sum(x, "cols"), "rows"), "tm")


def halve_scatter(q, axis, dim):
    n = lax.axis_size(axis)
    bits = n.bit_length() - 1
    here = lax.axis_index(axis)
    shape = q.shape
    q = q.reshape(shape[:dim] + (2,) * bits + shape[dim + 1 :])
    for level in range(bits):
        step = 1 << level
        at = dim + bits - 1 - level
        bit = (here // step) % 2
        keep = lax.dynamic_index_in_dim(q, bit, axis=at, keepdims=False)
        send = lax.dynamic_index_in_dim(q, 1 - bit, axis=at, keepdims=False)
        q = keep + lax.ppermute(send, axis, [(i, i ^ step) for i in range(n)])
    return q.reshape(shape[:dim] + (1,) + shape[dim + 1 :])


def xor_gather(x, axis):
    n = lax.axis_size(axis)
    here = lax.axis_index(axis)
    step = 1
    while step < n:
        other = lax.ppermute(x, axis, [(i, i ^ step) for i in range(n)])
        low = (here // step) % 2 == 0
        x = jnp.where(low, jnp.concatenate([x, other]), jnp.concatenate([other, x]))
        step *= 2
    return x


def six_gather(x, axis):
    n = lax.axis_size(axis)
    here = lax.axis_index(axis)
    other = lax.ppermute(x, axis, [(i, i ^ 1) for i in range(n)])
    x = jnp.where(here % 2 == 0, jnp.concatenate([x, other]), jnp.concatenate([other, x]))
    pair = here // 2
    ahead = lax.ppermute(x, axis, [(i, (i + 2) % n) for i in range(n)])
    behind = lax.ppermute(x, axis, [(i, (i + 4) % n) for i in range(n)])
    first = jnp.where(pair == 0, x, jnp.where(pair == 1, ahead, behind))
    second = jnp.where(pair == 1, x, jnp.where(pair == 2, ahead, behind))
    third = jnp.where(pair == 2, x, jnp.where(pair == 0, ahead, behind))
    return jnp.concatenate([first, second, third])


def six_scatter(q, axis):
    n = lax.axis_size(axis)
    here = lax.axis_index(axis)
    bit = here % 2
    pair = here // 2
    q = q.reshape((3, 2) + q.shape[1:])
    keep = lax.dynamic_index_in_dim(q, bit, axis=1, keepdims=False)
    send = lax.dynamic_index_in_dim(q, 1 - bit, axis=1, keepdims=False)
    q = keep + lax.ppermute(send, axis, [(i, i ^ 1) for i in range(n)])
    own = lax.dynamic_index_in_dim(q, pair, axis=0, keepdims=False)
    to_next = lax.dynamic_index_in_dim(q, (pair + 1) % 3, axis=0, keepdims=False)
    to_after = lax.dynamic_index_in_dim(q, (pair + 2) % 3, axis=0, keepdims=False)
    near = lax.ppermute(to_next, axis, [(i, (i + 2) % n) for i in range(n)])
    far = lax.ppermute(to_after, axis, [(i, (i + 4) % n) for i in range(n)])
    return own + near + far


def per_group(values):
    return jnp.repeat(values.reshape(GROUPS, -1).sum(axis=1), CH // GROUPS)


def to_pairs(field, pair_count, local_rows, local_cols, channels):
    paired = field.reshape(pair_count, 2, local_rows, local_cols, channels)
    return paired.transpose(0, 2, 3, 1, 4).reshape(pair_count, local_rows, local_cols, 2 * channels)


def from_pairs(field, local_rows, local_cols, channels):
    pair_count = field.shape[0]
    split = field.reshape(pair_count, local_rows + 2, local_cols + 2, 2, channels)
    return split.transpose(0, 3, 1, 2, 4).reshape(
        2 * pair_count, local_rows + 2, local_cols + 2, channels
    )


def per_device(video, cotangent, weight, gain, shift, conv_bias):
    local_frames, local_rows, local_cols, channels = video.shape
    pair_count = local_frames // 2
    packed = jnp.concatenate(
        [
            to_pairs(video, pair_count, local_rows, local_cols, channels),
            to_pairs(cotangent, pair_count, local_rows, local_cols, channels),
        ],
        axis=-1,
    )
    framed = padded_2(packed, (("tm", 0), ("rows", 1), ("cols", 2)), 1)
    video_ext = from_pairs(
        framed[: pair_count + 1, :, :, : 2 * channels], local_rows, local_cols, channels
    )
    grad_ext = from_pairs(framed[1:, :, :, 2 * channels :], local_rows, local_cols, channels)
    video_f = video.astype(jnp.float32)
    sums, squares = all_sum(
        jnp.stack([jnp.sum(video_f, axis=(0, 1, 2)), jnp.sum(video_f * video_f, axis=(0, 1, 2))])
    )
    devices_all = lax.axis_size("tm") * lax.axis_size("rows") * lax.axis_size("cols")
    count = float(local_frames * local_rows * local_cols * devices_all * (channels // GROUPS))
    mean_c = per_group(sums) / count
    variance = per_group(squares) / count - mean_c * mean_c
    rstd_c = lax.rsqrt(variance + 1e-06)
    normed_ext = (video_ext.astype(jnp.float32) - mean_c) * rstd_c
    pre_ext = normed_ext * gain + shift
    frame_pos = lax.broadcasted_iota(jnp.int32, (local_frames + 2, 1, 1, 1), 0)
    row_pos = lax.broadcasted_iota(jnp.int32, (1, local_rows + 2, 1, 1), 1)
    col_pos = lax.broadcasted_iota(jnp.int32, (1, 1, local_cols + 2, 1), 2)
    time_index = lax.axis_index("tm")
    row_index = lax.axis_index("rows")
    col_index = lax.axis_index("cols")
    valid = (frame_pos >= 2) | (time_index > 0)
    valid = (
        valid
        & ((row_pos > 0) | (row_index > 0))
        & ((row_pos < local_rows + 1) | (row_index < lax.axis_size("rows") - 1))
    )
    valid = (
        valid
        & ((col_pos > 0) | (col_index > 0))
        & ((col_pos < local_cols + 1) | (col_index < lax.axis_size("cols") - 1))
    )
    padded = jnp.where(valid, jax.nn.silu(pre_ext), 0.0).astype(jnp.bfloat16)
    whole = six_gather(xor_gather(weight, "cols"), "rows")
    cells = local_frames * local_rows * local_cols
    windows = []
    grad_windows = []
    for tap_t in range(3):
        for tap_r in range(3):
            for tap_c in range(3):
                windows.append(
                    padded[
                        tap_t : tap_t + local_frames,
                        tap_r : tap_r + local_rows,
                        tap_c : tap_c + local_cols,
                    ]
                )
                grad_windows.append(
                    grad_ext[
                        2 - tap_t : 2 - tap_t + local_frames,
                        2 - tap_r : 2 - tap_r + local_rows,
                        2 - tap_c : 2 - tap_c + local_cols,
                    ]
                )
    patches = jnp.concatenate(windows, axis=-1).reshape(cells, 27 * channels)
    grad_patches = jnp.concatenate(grad_windows, axis=-1).reshape(cells, 27 * channels)
    conv = jnp.dot(patches, whole, preferred_element_type=jnp.float32) + conv_bias
    output = (video_f + conv.reshape(local_frames, local_rows, local_cols, channels)).astype(
        jnp.bfloat16
    )
    grad_flat = cotangent.reshape(cells, channels)
    kernel_grad = lax.dot_general(
        patches, grad_flat, (((0,), (0,)), ((), ())), preferred_element_type=jnp.float32
    )
    flipped = (
        whole.reshape(27, channels, channels).transpose(0, 2, 1).reshape(27 * channels, channels)
    )
    grad_hidden = jnp.dot(grad_patches, flipped, preferred_element_type=jnp.float32).astype(
        jnp.bfloat16
    )
    grad_hidden = lax.optimization_barrier(grad_hidden).astype(jnp.float32)
    grad_hidden = grad_hidden.reshape(local_frames, local_rows, local_cols, channels)
    normed = normed_ext[2:, 1:-1, 1:-1]
    pre = pre_ext[2:, 1:-1, 1:-1]
    sigma = jax.nn.sigmoid(pre)
    grad_pre = grad_hidden * sigma * (1.0 + pre * (1.0 - sigma))
    grad_f = cotangent.astype(jnp.float32)
    gain_part = jnp.sum(grad_pre * normed, axis=(0, 1, 2))
    shift_part = jnp.sum(grad_pre, axis=(0, 1, 2))
    bias_part = jnp.sum(grad_f, axis=(0, 1, 2))
    grad_gain, grad_shift, grad_conv_bias = all_sum(jnp.stack([gain_part, shift_part, bias_part]))
    row_count = lax.axis_size("rows")
    col_count = lax.axis_size("cols")
    band = kernel_grad.reshape(row_count, col_count, -1, channels)
    band = halve_scatter(band, "cols", 1)
    band = six_scatter(band.reshape(row_count, -1, channels), "rows")
    grad_weight = xor_sum(band, "tm")
    term_a = per_group(gain * grad_shift) / count
    term_b = per_group(gain * grad_gain) / count
    grad_video = (grad_f + rstd_c * (grad_pre * gain - term_a - normed * term_b)).astype(
        jnp.bfloat16
    )
    return (output, grad_video, grad_weight, grad_gain, grad_shift, grad_conv_bias)


def solution(mesh):
    return jax.shard_map(
        per_device,
        mesh=mesh,
        in_specs=(
            P("tm", "rows", "cols", None),
            P("tm", "rows", "cols", None),
            P(("rows", "cols"), None),
            P(),
            P(),
            P(),
        ),
        out_specs=(
            P("tm", "rows", "cols", None),
            P("tm", "rows", "cols", None),
            P(("rows", "cols"), None),
            P(),
            P(),
            P(),
        ),
        check_vma=False,
    )
```

```python
import jax
import jax.numpy as jnp
from jax import lax
from jax.sharding import PartitionSpec as P

CH = 192
GROUPS = 32


def padded_2(block, sides, width):
    for axis, dim in sides:
        count = lax.axis_size(axis)
        forward = [(i, i + 1) for i in range(count - 1)]
        backward = [(target, source) for source, target in forward]
        low = lax.ppermute(
            lax.slice_in_dim(block, block.shape[dim] - width, None, axis=dim), axis, forward
        )
        high = lax.ppermute(lax.slice_in_dim(block, 0, width, axis=dim), axis, backward)
        block = jnp.concatenate([low, block, high], axis=dim)
    return block


def xor_sum(x, axis):
    n = lax.axis_size(axis)
    step = 1
    while step < n:
        x = x + lax.ppermute(x, axis, [(i, i ^ step) for i in range(n)])
        step *= 2
    return x


def six_sum(x, axis):
    n = lax.axis_size(axis)
    x = x + lax.ppermute(x, axis, [(i, i ^ 1) for i in range(n)])
    here = lax.axis_index(axis) // 2
    ahead = lax.ppermute(x, axis, [(i, (i + 2) % n) for i in range(n)])
    behind = lax.ppermute(x, axis, [(i, (i + 4) % n) for i in range(n)])
    first = jnp.where(here == 0, x, jnp.where(here == 1, ahead, behind))
    second = jnp.where(here == 1, x, jnp.where(here == 2, ahead, behind))
    third = jnp.where(here == 2, x, jnp.where(here == 0, ahead, behind))
    return (first + second) + third


def all_sum(x):
    return xor_sum(six_sum(xor_sum(x, "cols"), "rows"), "tm")


def halve_scatter(q, axis, dim):
    n = lax.axis_size(axis)
    bits = n.bit_length() - 1
    here = lax.axis_index(axis)
    shape = q.shape
    q = q.reshape(shape[:dim] + (2,) * bits + shape[dim + 1 :])
    for level in range(bits):
        step = 1 << level
        at = dim + bits - 1 - level
        bit = (here // step) % 2
        keep = lax.dynamic_index_in_dim(q, bit, axis=at, keepdims=False)
        send = lax.dynamic_index_in_dim(q, 1 - bit, axis=at, keepdims=False)
        q = keep + lax.ppermute(send, axis, [(i, i ^ step) for i in range(n)])
    return q.reshape(shape[:dim] + (1,) + shape[dim + 1 :])


def xor_gather(x, axis):
    n = lax.axis_size(axis)
    here = lax.axis_index(axis)
    step = 1
    while step < n:
        other = lax.ppermute(x, axis, [(i, i ^ step) for i in range(n)])
        low = (here // step) % 2 == 0
        x = jnp.where(low, jnp.concatenate([x, other]), jnp.concatenate([other, x]))
        step *= 2
    return x


def six_gather(x, axis):
    n = lax.axis_size(axis)
    here = lax.axis_index(axis)
    other = lax.ppermute(x, axis, [(i, i ^ 1) for i in range(n)])
    x = jnp.where(here % 2 == 0, jnp.concatenate([x, other]), jnp.concatenate([other, x]))
    pair = here // 2
    ahead = lax.ppermute(x, axis, [(i, (i + 2) % n) for i in range(n)])
    behind = lax.ppermute(x, axis, [(i, (i + 4) % n) for i in range(n)])
    first = jnp.where(pair == 0, x, jnp.where(pair == 1, ahead, behind))
    second = jnp.where(pair == 1, x, jnp.where(pair == 2, ahead, behind))
    third = jnp.where(pair == 2, x, jnp.where(pair == 0, ahead, behind))
    return jnp.concatenate([first, second, third])


def six_scatter(q, axis):
    n = lax.axis_size(axis)
    here = lax.axis_index(axis)
    bit = here % 2
    pair = here // 2
    q = q.reshape((3, 2) + q.shape[1:])
    keep = lax.dynamic_index_in_dim(q, bit, axis=1, keepdims=False)
    send = lax.dynamic_index_in_dim(q, 1 - bit, axis=1, keepdims=False)
    q = keep + lax.ppermute(send, axis, [(i, i ^ 1) for i in range(n)])
    own = lax.dynamic_index_in_dim(q, pair, axis=0, keepdims=False)
    to_next = lax.dynamic_index_in_dim(q, (pair + 1) % 3, axis=0, keepdims=False)
    to_after = lax.dynamic_index_in_dim(q, (pair + 2) % 3, axis=0, keepdims=False)
    near = lax.ppermute(to_next, axis, [(i, (i + 2) % n) for i in range(n)])
    far = lax.ppermute(to_after, axis, [(i, (i + 4) % n) for i in range(n)])
    return own + near + far


def three_way(here, mine, ahead, behind):
    first = jnp.where(here == 0, mine, jnp.where(here == 1, ahead, behind))
    second = jnp.where(here == 1, mine, jnp.where(here == 2, ahead, behind))
    third = jnp.where(here == 2, mine, jnp.where(here == 0, ahead, behind))
    return first, second, third


def stats_and_weight(stats, weight):
    count = lax.axis_size("cols")
    here = lax.axis_index("cols")
    step = 1
    while step < count:
        pairs = [(i, i ^ step) for i in range(count)]
        other_stats = lax.ppermute(stats, "cols", pairs)
        other_weight = lax.ppermute(weight, "cols", pairs)
        stats = stats + other_stats
        low = (here // step) % 2 == 0
        weight = jnp.where(
            low,
            jnp.concatenate([weight, other_weight]),
            jnp.concatenate([other_weight, weight]),
        )
        step *= 2
    count = lax.axis_size("rows")
    here = lax.axis_index("rows")
    pairs = [(i, i ^ 1) for i in range(count)]
    other_stats = lax.ppermute(stats, "rows", pairs)
    other_weight = lax.ppermute(weight, "rows", pairs)
    stats = stats + other_stats
    weight = jnp.where(
        here % 2 == 0,
        jnp.concatenate([weight, other_weight]),
        jnp.concatenate([other_weight, weight]),
    )
    ahead_pairs = [(i, (i + 2) % count) for i in range(count)]
    behind_pairs = [(i, (i + 4) % count) for i in range(count)]
    ahead_stats = lax.ppermute(stats, "rows", ahead_pairs)
    ahead_weight = lax.ppermute(weight, "rows", ahead_pairs)
    behind_stats = lax.ppermute(stats, "rows", behind_pairs)
    behind_weight = lax.ppermute(weight, "rows", behind_pairs)
    first, second, third = three_way(here // 2, stats, ahead_stats, behind_stats)
    stats = (first + second) + third
    weight = jnp.concatenate(three_way(here // 2, weight, ahead_weight, behind_weight))
    return xor_sum(stats, "tm"), weight


def reduce_grads(small, band):
    channels = small.shape[-1]
    extra = small.shape[0]
    count = lax.axis_size("cols")
    here = lax.axis_index("cols")
    bits = count.bit_length() - 1
    rows = band.shape[0]
    q = band.reshape((rows,) + (2,) * bits + band.shape[2:])
    for level in range(bits):
        step = 1 << level
        at = bits - level
        bit = (here // step) % 2
        keep = lax.dynamic_index_in_dim(q, bit, axis=at, keepdims=False)
        send = lax.dynamic_index_in_dim(q, 1 - bit, axis=at, keepdims=False)
        got = lax.ppermute(
            jnp.concatenate([send.reshape(-1, channels), small]),
            "cols",
            [(i, i ^ step) for i in range(count)],
        )
        q = keep + got[:-extra].reshape(keep.shape)
        small = small + got[-extra:]
    count = lax.axis_size("rows")
    here = lax.axis_index("rows")
    bit = here % 2
    pair = here // 2
    q = q.reshape((3, 2) + q.shape[1:])
    keep = lax.dynamic_index_in_dim(q, bit, axis=1, keepdims=False)
    send = lax.dynamic_index_in_dim(q, 1 - bit, axis=1, keepdims=False)
    got = lax.ppermute(
        jnp.concatenate([send.reshape(-1, channels), small]),
        "rows",
        [(i, i ^ 1) for i in range(count)],
    )
    q = keep + got[:-extra].reshape(keep.shape)
    small = small + got[-extra:]
    own = lax.dynamic_index_in_dim(q, pair, axis=0, keepdims=False)
    to_next = lax.dynamic_index_in_dim(q, (pair + 1) % 3, axis=0, keepdims=False)
    to_after = lax.dynamic_index_in_dim(q, (pair + 2) % 3, axis=0, keepdims=False)
    near = lax.ppermute(
        jnp.concatenate([to_next, small]), "rows", [(i, (i + 2) % count) for i in range(count)]
    )
    far = lax.ppermute(
        jnp.concatenate([to_after, small]), "rows", [(i, (i + 4) % count) for i in range(count)]
    )
    band = own + near[:-extra] + far[:-extra]
    first, second, third = three_way(pair, small, near[-extra:], far[-extra:])
    small = (first + second) + third
    both = xor_sum(jnp.concatenate([band, small]), "tm")
    return both[-extra:], both[:-extra]


def per_group(values):
    return jnp.repeat(values.reshape(GROUPS, -1).sum(axis=1), CH // GROUPS)


def to_pairs(field, pair_count, local_rows, local_cols, channels):
    paired = field.reshape(pair_count, 2, local_rows, local_cols, channels)
    return paired.transpose(0, 2, 3, 1, 4).reshape(pair_count, local_rows, local_cols, 2 * channels)


def from_pairs(field, local_rows, local_cols, channels):
    pair_count = field.shape[0]
    split = field.reshape(pair_count, local_rows + 2, local_cols + 2, 2, channels)
    return split.transpose(0, 3, 1, 2, 4).reshape(
        2 * pair_count, local_rows + 2, local_cols + 2, channels
    )


def per_device(video, cotangent, weight, gain, shift, conv_bias):
    local_frames, local_rows, local_cols, channels = video.shape
    pair_count = local_frames // 2
    packed = jnp.concatenate(
        [
            to_pairs(video, pair_count, local_rows, local_cols, channels),
            to_pairs(cotangent, pair_count, local_rows, local_cols, channels),
        ],
        axis=-1,
    )
    framed = padded_2(packed, (("tm", 0), ("rows", 1), ("cols", 2)), 1)
    video_ext = from_pairs(
        framed[: pair_count + 1, :, :, : 2 * channels], local_rows, local_cols, channels
    )
    grad_ext = from_pairs(framed[1:, :, :, 2 * channels :], local_rows, local_cols, channels)
    video_f = video.astype(jnp.float32)
    (sums, squares), whole = stats_and_weight(
        jnp.stack([jnp.sum(video_f, axis=(0, 1, 2)), jnp.sum(video_f * video_f, axis=(0, 1, 2))]),
        weight,
    )
    devices_all = lax.axis_size("tm") * lax.axis_size("rows") * lax.axis_size("cols")
    count = float(local_frames * local_rows * local_cols * devices_all * (channels // GROUPS))
    mean_c = per_group(sums) / count
    variance = per_group(squares) / count - mean_c * mean_c
    rstd_c = lax.rsqrt(variance + 1e-06)
    normed_ext = (video_ext.astype(jnp.float32) - mean_c) * rstd_c
    pre_ext = normed_ext * gain + shift
    frame_pos = lax.broadcasted_iota(jnp.int32, (local_frames + 2, 1, 1, 1), 0)
    row_pos = lax.broadcasted_iota(jnp.int32, (1, local_rows + 2, 1, 1), 1)
    col_pos = lax.broadcasted_iota(jnp.int32, (1, 1, local_cols + 2, 1), 2)
    time_index = lax.axis_index("tm")
    row_index = lax.axis_index("rows")
    col_index = lax.axis_index("cols")
    valid = (frame_pos >= 2) | (time_index > 0)
    valid = (
        valid
        & ((row_pos > 0) | (row_index > 0))
        & ((row_pos < local_rows + 1) | (row_index < lax.axis_size("rows") - 1))
    )
    valid = (
        valid
        & ((col_pos > 0) | (col_index > 0))
        & ((col_pos < local_cols + 1) | (col_index < lax.axis_size("cols") - 1))
    )
    padded = jnp.where(valid, jax.nn.silu(pre_ext), 0.0).astype(jnp.bfloat16)
    cells = local_frames * local_rows * local_cols
    windows = []
    grad_windows = []
    for tap_t in range(3):
        for tap_r in range(3):
            for tap_c in range(3):
                windows.append(
                    padded[
                        tap_t : tap_t + local_frames,
                        tap_r : tap_r + local_rows,
                        tap_c : tap_c + local_cols,
                    ]
                )
                grad_windows.append(
                    grad_ext[
                        2 - tap_t : 2 - tap_t + local_frames,
                        2 - tap_r : 2 - tap_r + local_rows,
                        2 - tap_c : 2 - tap_c + local_cols,
                    ]
                )
    patches = jnp.concatenate(windows, axis=-1).reshape(cells, 27 * channels)
    grad_patches = jnp.concatenate(grad_windows, axis=-1).reshape(cells, 27 * channels)
    conv = jnp.dot(patches, whole, preferred_element_type=jnp.float32) + conv_bias
    output = (video_f + conv.reshape(local_frames, local_rows, local_cols, channels)).astype(
        jnp.bfloat16
    )
    grad_flat = cotangent.reshape(cells, channels)
    kernel_grad = lax.dot_general(
        patches, grad_flat, (((0,), (0,)), ((), ())), preferred_element_type=jnp.float32
    )
    flipped = (
        whole.reshape(27, channels, channels).transpose(0, 2, 1).reshape(27 * channels, channels)
    )
    grad_hidden = jnp.dot(grad_patches, flipped, preferred_element_type=jnp.float32).astype(
        jnp.bfloat16
    )
    grad_hidden = lax.optimization_barrier(grad_hidden).astype(jnp.float32)
    grad_hidden = grad_hidden.reshape(local_frames, local_rows, local_cols, channels)
    normed = normed_ext[2:, 1:-1, 1:-1]
    pre = pre_ext[2:, 1:-1, 1:-1]
    sigma = jax.nn.sigmoid(pre)
    grad_pre = grad_hidden * sigma * (1.0 + pre * (1.0 - sigma))
    grad_f = cotangent.astype(jnp.float32)
    gain_part = jnp.sum(grad_pre * normed, axis=(0, 1, 2))
    shift_part = jnp.sum(grad_pre, axis=(0, 1, 2))
    bias_part = jnp.sum(grad_f, axis=(0, 1, 2))
    row_count = lax.axis_size("rows")
    col_count = lax.axis_size("cols")
    (grad_gain, grad_shift, grad_conv_bias), grad_weight = reduce_grads(
        jnp.stack([gain_part, shift_part, bias_part]),
        kernel_grad.reshape(row_count, col_count, -1, channels),
    )
    term_a = per_group(gain * grad_shift) / count
    term_b = per_group(gain * grad_gain) / count
    grad_video = (grad_f + rstd_c * (grad_pre * gain - term_a - normed * term_b)).astype(
        jnp.bfloat16
    )
    return (output, grad_video, grad_weight, grad_gain, grad_shift, grad_conv_bias)


def solution(mesh):
    return jax.shard_map(
        per_device,
        mesh=mesh,
        in_specs=(
            P("tm", "rows", "cols", None),
            P("tm", "rows", "cols", None),
            P(("rows", "cols"), None),
            P(),
            P(),
            P(),
        ),
        out_specs=(
            P("tm", "rows", "cols", None),
            P("tm", "rows", "cols", None),
            P(("rows", "cols"), None),
            P(),
            P(),
            P(),
        ),
        check_vma=False,
    )
```

```python
import jax
import jax.numpy as jnp
from jax import lax
from jax.sharding import PartitionSpec as P

CH = 192
GROUPS = 32


def padded_2(block, sides, width):
    for axis, dim in sides:
        count = lax.axis_size(axis)
        forward = [(i, i + 1) for i in range(count - 1)]
        backward = [(target, source) for source, target in forward]
        low = lax.ppermute(
            lax.slice_in_dim(block, block.shape[dim] - width, None, axis=dim), axis, forward
        )
        high = lax.ppermute(lax.slice_in_dim(block, 0, width, axis=dim), axis, backward)
        block = jnp.concatenate([low, block, high], axis=dim)
    return block


def xor_sum(x, axis):
    n = lax.axis_size(axis)
    step = 1
    while step < n:
        x = x + lax.ppermute(x, axis, [(i, i ^ step) for i in range(n)])
        step *= 2
    return x


def six_sum(x, axis):
    n = lax.axis_size(axis)
    x = x + lax.ppermute(x, axis, [(i, i ^ 1) for i in range(n)])
    here = lax.axis_index(axis) // 2
    ahead = lax.ppermute(x, axis, [(i, (i + 2) % n) for i in range(n)])
    behind = lax.ppermute(x, axis, [(i, (i + 4) % n) for i in range(n)])
    first = jnp.where(here == 0, x, jnp.where(here == 1, ahead, behind))
    second = jnp.where(here == 1, x, jnp.where(here == 2, ahead, behind))
    third = jnp.where(here == 2, x, jnp.where(here == 0, ahead, behind))
    return (first + second) + third


def all_sum(x):
    return xor_sum(six_sum(xor_sum(x, "cols"), "rows"), "tm")


def halve_scatter(q, axis, dim):
    n = lax.axis_size(axis)
    bits = n.bit_length() - 1
    here = lax.axis_index(axis)
    shape = q.shape
    q = q.reshape(shape[:dim] + (2,) * bits + shape[dim + 1 :])
    for level in range(bits):
        step = 1 << level
        at = dim + bits - 1 - level
        bit = (here // step) % 2
        keep = lax.dynamic_index_in_dim(q, bit, axis=at, keepdims=False)
        send = lax.dynamic_index_in_dim(q, 1 - bit, axis=at, keepdims=False)
        q = keep + lax.ppermute(send, axis, [(i, i ^ step) for i in range(n)])
    return q.reshape(shape[:dim] + (1,) + shape[dim + 1 :])


def xor_gather(x, axis):
    n = lax.axis_size(axis)
    here = lax.axis_index(axis)
    step = 1
    while step < n:
        other = lax.ppermute(x, axis, [(i, i ^ step) for i in range(n)])
        low = (here // step) % 2 == 0
        x = jnp.where(low, jnp.concatenate([x, other]), jnp.concatenate([other, x]))
        step *= 2
    return x


def six_gather(x, axis):
    n = lax.axis_size(axis)
    here = lax.axis_index(axis)
    other = lax.ppermute(x, axis, [(i, i ^ 1) for i in range(n)])
    x = jnp.where(here % 2 == 0, jnp.concatenate([x, other]), jnp.concatenate([other, x]))
    pair = here // 2
    ahead = lax.ppermute(x, axis, [(i, (i + 2) % n) for i in range(n)])
    behind = lax.ppermute(x, axis, [(i, (i + 4) % n) for i in range(n)])
    first = jnp.where(pair == 0, x, jnp.where(pair == 1, ahead, behind))
    second = jnp.where(pair == 1, x, jnp.where(pair == 2, ahead, behind))
    third = jnp.where(pair == 2, x, jnp.where(pair == 0, ahead, behind))
    return jnp.concatenate([first, second, third])


def six_scatter(q, axis):
    n = lax.axis_size(axis)
    here = lax.axis_index(axis)
    bit = here % 2
    pair = here // 2
    q = q.reshape((3, 2) + q.shape[1:])
    keep = lax.dynamic_index_in_dim(q, bit, axis=1, keepdims=False)
    send = lax.dynamic_index_in_dim(q, 1 - bit, axis=1, keepdims=False)
    q = keep + lax.ppermute(send, axis, [(i, i ^ 1) for i in range(n)])
    own = lax.dynamic_index_in_dim(q, pair, axis=0, keepdims=False)
    to_next = lax.dynamic_index_in_dim(q, (pair + 1) % 3, axis=0, keepdims=False)
    to_after = lax.dynamic_index_in_dim(q, (pair + 2) % 3, axis=0, keepdims=False)
    near = lax.ppermute(to_next, axis, [(i, (i + 2) % n) for i in range(n)])
    far = lax.ppermute(to_after, axis, [(i, (i + 4) % n) for i in range(n)])
    return own + near + far


def three_way(here, mine, ahead, behind):
    first = jnp.where(here == 0, mine, jnp.where(here == 1, ahead, behind))
    second = jnp.where(here == 1, mine, jnp.where(here == 2, ahead, behind))
    third = jnp.where(here == 2, mine, jnp.where(here == 0, ahead, behind))
    return first, second, third


def split_high(x):
    scaled = x * 65537.0
    return scaled - (scaled - x)


def to_pieces(x):
    high = split_high(x)
    rest = x - high
    middle = split_high(rest)
    return jnp.concatenate([high, middle, rest - middle]).astype(jnp.bfloat16)


def from_pieces(pieces):
    high, middle, low = jnp.split(pieces.astype(jnp.float32), 3)
    return (high + middle) + low


def stats_and_weight(stats, weight):
    extra = 3 * stats.shape[0]

    def swap(weight, stats, axis, pairs):
        got = lax.ppermute(jnp.concatenate([weight, to_pieces(stats)]), axis, pairs)
        return got[:-extra], from_pieces(got[-extra:])

    count = lax.axis_size("cols")
    here = lax.axis_index("cols")
    step = 1
    while step < count:
        other_weight, other_stats = swap(weight, stats, "cols", [(i, i ^ step) for i in range(count)])
        stats = stats + other_stats
        low = (here // step) % 2 == 0
        weight = jnp.where(
            low,
            jnp.concatenate([weight, other_weight]),
            jnp.concatenate([other_weight, weight]),
        )
        step *= 2
    count = lax.axis_size("rows")
    here = lax.axis_index("rows")
    other_weight, other_stats = swap(weight, stats, "rows", [(i, i ^ 1) for i in range(count)])
    stats = stats + other_stats
    weight = jnp.where(
        here % 2 == 0,
        jnp.concatenate([weight, other_weight]),
        jnp.concatenate([other_weight, weight]),
    )
    ahead_weight, ahead_stats = swap(
        weight, stats, "rows", [(i, (i + 2) % count) for i in range(count)]
    )
    behind_weight, behind_stats = swap(
        weight, stats, "rows", [(i, (i + 4) % count) for i in range(count)]
    )
    first, second, third = three_way(here // 2, stats, ahead_stats, behind_stats)
    stats = (first + second) + third
    weight = jnp.concatenate(three_way(here // 2, weight, ahead_weight, behind_weight))
    return xor_sum(stats, "tm"), weight


def reduce_grads(small, band):
    channels = small.shape[-1]
    extra = small.shape[0]
    count = lax.axis_size("cols")
    here = lax.axis_index("cols")
    bits = count.bit_length() - 1
    rows = band.shape[0]
    q = band.reshape((rows,) + (2,) * bits + band.shape[2:])
    for level in range(bits):
        step = 1 << level
        at = bits - level
        bit = (here // step) % 2
        keep = lax.dynamic_index_in_dim(q, bit, axis=at, keepdims=False)
        send = lax.dynamic_index_in_dim(q, 1 - bit, axis=at, keepdims=False)
        got = lax.ppermute(
            jnp.concatenate([send.reshape(-1, channels), small]),
            "cols",
            [(i, i ^ step) for i in range(count)],
        )
        q = keep + got[:-extra].reshape(keep.shape)
        small = small + got[-extra:]
    count = lax.axis_size("rows")
    here = lax.axis_index("rows")
    bit = here % 2
    pair = here // 2
    q = q.reshape((3, 2) + q.shape[1:])
    keep = lax.dynamic_index_in_dim(q, bit, axis=1, keepdims=False)
    send = lax.dynamic_index_in_dim(q, 1 - bit, axis=1, keepdims=False)
    got = lax.ppermute(
        jnp.concatenate([send.reshape(-1, channels), small]),
        "rows",
        [(i, i ^ 1) for i in range(count)],
    )
    q = keep + got[:-extra].reshape(keep.shape)
    small = small + got[-extra:]
    own = lax.dynamic_index_in_dim(q, pair, axis=0, keepdims=False)
    to_next = lax.dynamic_index_in_dim(q, (pair + 1) % 3, axis=0, keepdims=False)
    to_after = lax.dynamic_index_in_dim(q, (pair + 2) % 3, axis=0, keepdims=False)
    near = lax.ppermute(
        jnp.concatenate([to_next, small]), "rows", [(i, (i + 2) % count) for i in range(count)]
    )
    far = lax.ppermute(
        jnp.concatenate([to_after, small]), "rows", [(i, (i + 4) % count) for i in range(count)]
    )
    band = own + near[:-extra] + far[:-extra]
    first, second, third = three_way(pair, small, near[-extra:], far[-extra:])
    small = (first + second) + third
    both = xor_sum(jnp.concatenate([band, small]), "tm")
    return both[-extra:], both[:-extra]


def per_group(values):
    return jnp.repeat(values.reshape(GROUPS, -1).sum(axis=1), CH // GROUPS)


def to_pairs(field, pair_count, local_rows, local_cols, channels):
    paired = field.reshape(pair_count, 2, local_rows, local_cols, channels)
    return paired.transpose(0, 2, 3, 1, 4).reshape(pair_count, local_rows, local_cols, 2 * channels)


def from_pairs(field, local_rows, local_cols, channels):
    pair_count = field.shape[0]
    split = field.reshape(pair_count, local_rows + 2, local_cols + 2, 2, channels)
    return split.transpose(0, 3, 1, 2, 4).reshape(
        2 * pair_count, local_rows + 2, local_cols + 2, channels
    )


def per_device(video, cotangent, weight, gain, shift, conv_bias):
    local_frames, local_rows, local_cols, channels = video.shape
    pair_count = local_frames // 2
    packed = jnp.concatenate(
        [
            to_pairs(video, pair_count, local_rows, local_cols, channels),
            to_pairs(cotangent, pair_count, local_rows, local_cols, channels),
        ],
        axis=-1,
    )
    framed = padded_2(packed, (("tm", 0), ("rows", 1), ("cols", 2)), 1)
    video_ext = from_pairs(
        framed[: pair_count + 1, :, :, : 2 * channels], local_rows, local_cols, channels
    )
    grad_ext = from_pairs(framed[1:, :, :, 2 * channels :], local_rows, local_cols, channels)
    video_f = video.astype(jnp.float32)
    (sums, squares), whole = stats_and_weight(
        jnp.stack([jnp.sum(video_f, axis=(0, 1, 2)), jnp.sum(video_f * video_f, axis=(0, 1, 2))]),
        weight,
    )
    devices_all = lax.axis_size("tm") * lax.axis_size("rows") * lax.axis_size("cols")
    count = float(local_frames * local_rows * local_cols * devices_all * (channels // GROUPS))
    mean_c = per_group(sums) / count
    variance = per_group(squares) / count - mean_c * mean_c
    rstd_c = lax.rsqrt(variance + 1e-06)
    normed_ext = (video_ext.astype(jnp.float32) - mean_c) * rstd_c
    pre_ext = normed_ext * gain + shift
    frame_pos = lax.broadcasted_iota(jnp.int32, (local_frames + 2, 1, 1, 1), 0)
    row_pos = lax.broadcasted_iota(jnp.int32, (1, local_rows + 2, 1, 1), 1)
    col_pos = lax.broadcasted_iota(jnp.int32, (1, 1, local_cols + 2, 1), 2)
    time_index = lax.axis_index("tm")
    row_index = lax.axis_index("rows")
    col_index = lax.axis_index("cols")
    valid = (frame_pos >= 2) | (time_index > 0)
    valid = (
        valid
        & ((row_pos > 0) | (row_index > 0))
        & ((row_pos < local_rows + 1) | (row_index < lax.axis_size("rows") - 1))
    )
    valid = (
        valid
        & ((col_pos > 0) | (col_index > 0))
        & ((col_pos < local_cols + 1) | (col_index < lax.axis_size("cols") - 1))
    )
    padded = jnp.where(valid, jax.nn.silu(pre_ext), 0.0).astype(jnp.bfloat16)
    cells = local_frames * local_rows * local_cols
    windows = []
    grad_windows = []
    for tap_t in range(3):
        for tap_r in range(3):
            for tap_c in range(3):
                windows.append(
                    padded[
                        tap_t : tap_t + local_frames,
                        tap_r : tap_r + local_rows,
                        tap_c : tap_c + local_cols,
                    ]
                )
                grad_windows.append(
                    grad_ext[
                        2 - tap_t : 2 - tap_t + local_frames,
                        2 - tap_r : 2 - tap_r + local_rows,
                        2 - tap_c : 2 - tap_c + local_cols,
                    ]
                )
    patches = jnp.concatenate(windows, axis=-1).reshape(cells, 27 * channels)
    grad_patches = jnp.concatenate(grad_windows, axis=-1).reshape(cells, 27 * channels)
    conv = jnp.dot(patches, whole, preferred_element_type=jnp.float32) + conv_bias
    output = (video_f + conv.reshape(local_frames, local_rows, local_cols, channels)).astype(
        jnp.bfloat16
    )
    grad_flat = cotangent.reshape(cells, channels)
    kernel_grad = lax.dot_general(
        patches, grad_flat, (((0,), (0,)), ((), ())), preferred_element_type=jnp.float32
    )
    flipped = (
        whole.reshape(27, channels, channels).transpose(0, 2, 1).reshape(27 * channels, channels)
    )
    grad_hidden = jnp.dot(grad_patches, flipped, preferred_element_type=jnp.float32).astype(
        jnp.bfloat16
    )
    grad_hidden = lax.optimization_barrier(grad_hidden).astype(jnp.float32)
    grad_hidden = grad_hidden.reshape(local_frames, local_rows, local_cols, channels)
    normed = normed_ext[2:, 1:-1, 1:-1]
    pre = pre_ext[2:, 1:-1, 1:-1]
    sigma = jax.nn.sigmoid(pre)
    grad_pre = grad_hidden * sigma * (1.0 + pre * (1.0 - sigma))
    grad_f = cotangent.astype(jnp.float32)
    gain_part = jnp.sum(grad_pre * normed, axis=(0, 1, 2))
    shift_part = jnp.sum(grad_pre, axis=(0, 1, 2))
    bias_part = jnp.sum(grad_f, axis=(0, 1, 2))
    row_count = lax.axis_size("rows")
    col_count = lax.axis_size("cols")
    (grad_gain, grad_shift, grad_conv_bias), grad_weight = reduce_grads(
        jnp.stack([gain_part, shift_part, bias_part]),
        kernel_grad.reshape(row_count, col_count, -1, channels),
    )
    term_a = per_group(gain * grad_shift) / count
    term_b = per_group(gain * grad_gain) / count
    grad_video = (grad_f + rstd_c * (grad_pre * gain - term_a - normed * term_b)).astype(
        jnp.bfloat16
    )
    return (output, grad_video, grad_weight, grad_gain, grad_shift, grad_conv_bias)


def solution(mesh):
    return jax.shard_map(
        per_device,
        mesh=mesh,
        in_specs=(
            P("tm", "rows", "cols", None),
            P("tm", "rows", "cols", None),
            P(("rows", "cols"), None),
            P(),
            P(),
            P(),
        ),
        out_specs=(
            P("tm", "rows", "cols", None),
            P("tm", "rows", "cols", None),
            P(("rows", "cols"), None),
            P(),
            P(),
            P(),
        ),
        check_vma=False,
    )
```

```python
import jax
import jax.numpy as jnp
from jax import lax
from jax.sharding import PartitionSpec as P

CH = 192
GROUPS = 32


def padded_2(block, sides, width):
    for axis, dim in sides:
        count = lax.axis_size(axis)
        forward = [(i, i + 1) for i in range(count - 1)]
        backward = [(target, source) for source, target in forward]
        low = lax.ppermute(
            lax.slice_in_dim(block, block.shape[dim] - width, None, axis=dim), axis, forward
        )
        high = lax.ppermute(lax.slice_in_dim(block, 0, width, axis=dim), axis, backward)
        block = jnp.concatenate([low, block, high], axis=dim)
    return block


def xor_sum(x, axis):
    n = lax.axis_size(axis)
    step = 1
    while step < n:
        x = x + lax.ppermute(x, axis, [(i, i ^ step) for i in range(n)])
        step *= 2
    return x


def six_sum(x, axis):
    n = lax.axis_size(axis)
    x = x + lax.ppermute(x, axis, [(i, i ^ 1) for i in range(n)])
    here = lax.axis_index(axis) // 2
    ahead = lax.ppermute(x, axis, [(i, (i + 2) % n) for i in range(n)])
    behind = lax.ppermute(x, axis, [(i, (i + 4) % n) for i in range(n)])
    first = jnp.where(here == 0, x, jnp.where(here == 1, ahead, behind))
    second = jnp.where(here == 1, x, jnp.where(here == 2, ahead, behind))
    third = jnp.where(here == 2, x, jnp.where(here == 0, ahead, behind))
    return (first + second) + third


def all_sum(x):
    return xor_sum(six_sum(xor_sum(x, "cols"), "rows"), "tm")


def halve_scatter(q, axis, dim):
    n = lax.axis_size(axis)
    bits = n.bit_length() - 1
    here = lax.axis_index(axis)
    shape = q.shape
    q = q.reshape(shape[:dim] + (2,) * bits + shape[dim + 1 :])
    for level in range(bits):
        step = 1 << level
        at = dim + bits - 1 - level
        bit = (here // step) % 2
        keep = lax.dynamic_index_in_dim(q, bit, axis=at, keepdims=False)
        send = lax.dynamic_index_in_dim(q, 1 - bit, axis=at, keepdims=False)
        q = keep + lax.ppermute(send, axis, [(i, i ^ step) for i in range(n)])
    return q.reshape(shape[:dim] + (1,) + shape[dim + 1 :])


def six_scatter(q, axis):
    n = lax.axis_size(axis)
    here = lax.axis_index(axis)
    bit = here % 2
    pair = here // 2
    q = q.reshape((3, 2) + q.shape[1:])
    keep = lax.dynamic_index_in_dim(q, bit, axis=1, keepdims=False)
    send = lax.dynamic_index_in_dim(q, 1 - bit, axis=1, keepdims=False)
    q = keep + lax.ppermute(send, axis, [(i, i ^ 1) for i in range(n)])
    own = lax.dynamic_index_in_dim(q, pair, axis=0, keepdims=False)
    to_next = lax.dynamic_index_in_dim(q, (pair + 1) % 3, axis=0, keepdims=False)
    to_after = lax.dynamic_index_in_dim(q, (pair + 2) % 3, axis=0, keepdims=False)
    near = lax.ppermute(to_next, axis, [(i, (i + 2) % n) for i in range(n)])
    far = lax.ppermute(to_after, axis, [(i, (i + 4) % n) for i in range(n)])
    return own + near + far


def per_group(values):
    return jnp.repeat(values.reshape(GROUPS, -1).sum(axis=1), CH // GROUPS)


def to_pairs(field, pair_count, local_rows, local_cols, channels):
    paired = field.reshape(pair_count, 2, local_rows, local_cols, channels)
    return paired.transpose(0, 2, 3, 1, 4).reshape(pair_count, local_rows, local_cols, 2 * channels)


def from_pairs(field, local_rows, local_cols, channels):
    pair_count = field.shape[0]
    split = field.reshape(pair_count, local_rows + 2, local_cols + 2, 2, channels)
    return split.transpose(0, 3, 1, 2, 4).reshape(
        2 * pair_count, local_rows + 2, local_cols + 2, channels
    )


def per_device(video, cotangent, weight, gain, shift, conv_bias):
    local_frames, local_rows, local_cols, channels = video.shape
    pair_count = local_frames // 2
    packed = jnp.concatenate(
        [
            to_pairs(video, pair_count, local_rows, local_cols, channels),
            to_pairs(cotangent, pair_count, local_rows, local_cols, channels),
        ],
        axis=-1,
    )
    framed = padded_2(packed, (("tm", 0), ("rows", 1), ("cols", 2)), 1)
    video_ext = from_pairs(
        framed[: pair_count + 1, :, :, : 2 * channels], local_rows, local_cols, channels
    )
    grad_ext = from_pairs(framed[1:, :, :, 2 * channels :], local_rows, local_cols, channels)
    video_f = video.astype(jnp.float32)
    sums, squares = all_sum(
        jnp.stack([jnp.sum(video_f, axis=(0, 1, 2)), jnp.sum(video_f * video_f, axis=(0, 1, 2))])
    )
    devices_all = lax.axis_size("tm") * lax.axis_size("rows") * lax.axis_size("cols")
    count = float(local_frames * local_rows * local_cols * devices_all * (channels // GROUPS))
    mean_c = per_group(sums) / count
    variance = per_group(squares) / count - mean_c * mean_c
    rstd_c = lax.rsqrt(variance + 1e-06)
    normed_ext = (video_ext.astype(jnp.float32) - mean_c) * rstd_c
    pre_ext = normed_ext * gain + shift
    frame_pos = lax.broadcasted_iota(jnp.int32, (local_frames + 2, 1, 1, 1), 0)
    row_pos = lax.broadcasted_iota(jnp.int32, (1, local_rows + 2, 1, 1), 1)
    col_pos = lax.broadcasted_iota(jnp.int32, (1, 1, local_cols + 2, 1), 2)
    time_index = lax.axis_index("tm")
    row_index = lax.axis_index("rows")
    col_index = lax.axis_index("cols")
    valid = (frame_pos >= 2) | (time_index > 0)
    valid = (
        valid
        & ((row_pos > 0) | (row_index > 0))
        & ((row_pos < local_rows + 1) | (row_index < lax.axis_size("rows") - 1))
    )
    valid = (
        valid
        & ((col_pos > 0) | (col_index > 0))
        & ((col_pos < local_cols + 1) | (col_index < lax.axis_size("cols") - 1))
    )
    padded = jnp.where(valid, jax.nn.silu(pre_ext), 0.0).astype(jnp.bfloat16)
    whole = lax.all_gather(weight, ("rows", "cols"), axis=0, tiled=True)
    cells = local_frames * local_rows * local_cols
    windows = []
    grad_windows = []
    for tap_t in range(3):
        for tap_r in range(3):
            for tap_c in range(3):
                windows.append(
                    padded[
                        tap_t : tap_t + local_frames,
                        tap_r : tap_r + local_rows,
                        tap_c : tap_c + local_cols,
                    ]
                )
                grad_windows.append(
                    grad_ext[
                        2 - tap_t : 2 - tap_t + local_frames,
                        2 - tap_r : 2 - tap_r + local_rows,
                        2 - tap_c : 2 - tap_c + local_cols,
                    ]
                )
    patches = jnp.concatenate(windows, axis=-1).reshape(cells, 27 * channels)
    grad_patches = jnp.concatenate(grad_windows, axis=-1).reshape(cells, 27 * channels)
    conv = jnp.dot(patches, whole, preferred_element_type=jnp.float32) + conv_bias
    output = (video_f + conv.reshape(local_frames, local_rows, local_cols, channels)).astype(
        jnp.bfloat16
    )
    grad_flat = cotangent.reshape(cells, channels)
    kernel_grad = lax.dot_general(
        patches, grad_flat, (((0,), (0,)), ((), ())), preferred_element_type=jnp.float32
    )
    flipped = (
        whole.reshape(27, channels, channels).transpose(0, 2, 1).reshape(27 * channels, channels)
    )
    grad_hidden = jnp.dot(grad_patches, flipped, preferred_element_type=jnp.float32).astype(
        jnp.bfloat16
    )
    grad_hidden = lax.optimization_barrier(grad_hidden).astype(jnp.float32)
    grad_hidden = grad_hidden.reshape(local_frames, local_rows, local_cols, channels)
    normed = normed_ext[2:, 1:-1, 1:-1]
    pre = pre_ext[2:, 1:-1, 1:-1]
    sigma = jax.nn.sigmoid(pre)
    grad_pre = grad_hidden * sigma * (1.0 + pre * (1.0 - sigma))
    grad_f = cotangent.astype(jnp.float32)
    gain_part = jnp.sum(grad_pre * normed, axis=(0, 1, 2))
    shift_part = jnp.sum(grad_pre, axis=(0, 1, 2))
    bias_part = jnp.sum(grad_f, axis=(0, 1, 2))
    grad_gain, grad_shift, grad_conv_bias = all_sum(jnp.stack([gain_part, shift_part, bias_part]))
    row_count = lax.axis_size("rows")
    col_count = lax.axis_size("cols")
    band = kernel_grad.reshape(row_count, col_count, -1, channels)
    band = halve_scatter(band, "cols", 1)
    band = six_scatter(band.reshape(row_count, -1, channels), "rows")
    grad_weight = xor_sum(band, "tm")
    term_a = per_group(gain * grad_shift) / count
    term_b = per_group(gain * grad_gain) / count
    grad_video = (grad_f + rstd_c * (grad_pre * gain - term_a - normed * term_b)).astype(
        jnp.bfloat16
    )
    return (output, grad_video, grad_weight, grad_gain, grad_shift, grad_conv_bias)


def solution(mesh):
    return jax.shard_map(
        per_device,
        mesh=mesh,
        in_specs=(
            P("tm", "rows", "cols", None),
            P("tm", "rows", "cols", None),
            P(("rows", "cols"), None),
            P(),
            P(),
            P(),
        ),
        out_specs=(
            P("tm", "rows", "cols", None),
            P("tm", "rows", "cols", None),
            P(("rows", "cols"), None),
            P(),
            P(),
            P(),
        ),
        check_vma=False,
    )
```

```python
import jax
import jax.numpy as jnp
from jax import lax
from jax.sharding import PartitionSpec as P

CH = 192
GROUPS = 32


def padded_2(block, sides, width):
    for axis, dim in sides:
        count = lax.axis_size(axis)
        forward = [(i, i + 1) for i in range(count - 1)]
        backward = [(target, source) for source, target in forward]
        low = lax.ppermute(
            lax.slice_in_dim(block, block.shape[dim] - width, None, axis=dim), axis, forward
        )
        high = lax.ppermute(lax.slice_in_dim(block, 0, width, axis=dim), axis, backward)
        block = jnp.concatenate([low, block, high], axis=dim)
    return block


def xor_sum(x, axis):
    n = lax.axis_size(axis)
    step = 1
    while step < n:
        x = x + lax.ppermute(x, axis, [(i, i ^ step) for i in range(n)])
        step *= 2
    return x


def six_sum(x, axis):
    n = lax.axis_size(axis)
    x = x + lax.ppermute(x, axis, [(i, i ^ 1) for i in range(n)])
    here = lax.axis_index(axis) // 2
    ahead = lax.ppermute(x, axis, [(i, (i + 2) % n) for i in range(n)])
    behind = lax.ppermute(x, axis, [(i, (i + 4) % n) for i in range(n)])
    first = jnp.where(here == 0, x, jnp.where(here == 1, ahead, behind))
    second = jnp.where(here == 1, x, jnp.where(here == 2, ahead, behind))
    third = jnp.where(here == 2, x, jnp.where(here == 0, ahead, behind))
    return (first + second) + third


def all_sum(x):
    return xor_sum(six_sum(xor_sum(x, "cols"), "rows"), "tm")


def halve_scatter(q, axis, dim):
    n = lax.axis_size(axis)
    bits = n.bit_length() - 1
    here = lax.axis_index(axis)
    shape = q.shape
    q = q.reshape(shape[:dim] + (2,) * bits + shape[dim + 1 :])
    for level in range(bits):
        step = 1 << level
        at = dim + bits - 1 - level
        bit = (here // step) % 2
        keep = lax.dynamic_index_in_dim(q, bit, axis=at, keepdims=False)
        send = lax.dynamic_index_in_dim(q, 1 - bit, axis=at, keepdims=False)
        q = keep + lax.ppermute(send, axis, [(i, i ^ step) for i in range(n)])
    return q.reshape(shape[:dim] + (1,) + shape[dim + 1 :])


def six_scatter(q, axis):
    n = lax.axis_size(axis)
    here = lax.axis_index(axis)
    bit = here % 2
    pair = here // 2
    q = q.reshape((3, 2) + q.shape[1:])
    keep = lax.dynamic_index_in_dim(q, bit, axis=1, keepdims=False)
    send = lax.dynamic_index_in_dim(q, 1 - bit, axis=1, keepdims=False)
    q = keep + lax.ppermute(send, axis, [(i, i ^ 1) for i in range(n)])
    own = lax.dynamic_index_in_dim(q, pair, axis=0, keepdims=False)
    to_next = lax.dynamic_index_in_dim(q, (pair + 1) % 3, axis=0, keepdims=False)
    to_after = lax.dynamic_index_in_dim(q, (pair + 2) % 3, axis=0, keepdims=False)
    near = lax.ppermute(to_next, axis, [(i, (i + 2) % n) for i in range(n)])
    far = lax.ppermute(to_after, axis, [(i, (i + 4) % n) for i in range(n)])
    return own + near + far


def per_group(values):
    return jnp.repeat(values.reshape(GROUPS, -1).sum(axis=1), CH // GROUPS)


def to_pairs(field, pair_count, local_rows, local_cols, channels):
    paired = field.reshape(pair_count, 2, local_rows, local_cols, channels)
    return paired.transpose(0, 2, 3, 1, 4).reshape(pair_count, local_rows, local_cols, 2 * channels)


def from_pairs(field, local_rows, local_cols, channels):
    pair_count = field.shape[0]
    split = field.reshape(pair_count, local_rows + 2, local_cols + 2, 2, channels)
    return split.transpose(0, 3, 1, 2, 4).reshape(
        2 * pair_count, local_rows + 2, local_cols + 2, channels
    )


def per_device(video, cotangent, weight, gain, shift, conv_bias):
    local_frames, local_rows, local_cols, channels = video.shape
    pair_count = local_frames // 2
    packed = jnp.concatenate(
        [
            to_pairs(video, pair_count, local_rows, local_cols, channels),
            to_pairs(cotangent, pair_count, local_rows, local_cols, channels),
        ],
        axis=-1,
    )
    framed = padded_2(packed, (("tm", 0), ("rows", 1), ("cols", 2)), 1)
    video_ext = from_pairs(
        framed[: pair_count + 1, :, :, : 2 * channels], local_rows, local_cols, channels
    )
    grad_ext = from_pairs(framed[1:, :, :, 2 * channels :], local_rows, local_cols, channels)
    video_f = video.astype(jnp.float32)
    sums, squares = all_sum(
        jnp.stack([jnp.sum(video_f, axis=(0, 1, 2)), jnp.sum(video_f * video_f, axis=(0, 1, 2))])
    )
    devices_all = lax.axis_size("tm") * lax.axis_size("rows") * lax.axis_size("cols")
    count = float(local_frames * local_rows * local_cols * devices_all * (channels // GROUPS))
    mean_c = per_group(sums) / count
    variance = per_group(squares) / count - mean_c * mean_c
    rstd_c = lax.rsqrt(variance + 1e-06)
    normed_ext = (video_ext.astype(jnp.float32) - mean_c) * rstd_c
    pre_ext = normed_ext * gain + shift
    frame_pos = lax.broadcasted_iota(jnp.int32, (local_frames + 2, 1, 1, 1), 0)
    row_pos = lax.broadcasted_iota(jnp.int32, (1, local_rows + 2, 1, 1), 1)
    col_pos = lax.broadcasted_iota(jnp.int32, (1, 1, local_cols + 2, 1), 2)
    time_index = lax.axis_index("tm")
    row_index = lax.axis_index("rows")
    col_index = lax.axis_index("cols")
    valid = (frame_pos >= 2) | (time_index > 0)
    valid = (
        valid
        & ((row_pos > 0) | (row_index > 0))
        & ((row_pos < local_rows + 1) | (row_index < lax.axis_size("rows") - 1))
    )
    valid = (
        valid
        & ((col_pos > 0) | (col_index > 0))
        & ((col_pos < local_cols + 1) | (col_index < lax.axis_size("cols") - 1))
    )
    padded = jnp.where(valid, jax.nn.silu(pre_ext), 0.0).astype(jnp.bfloat16)
    whole = lax.all_gather(
        lax.all_gather(weight, "cols", axis=0, tiled=True), "rows", axis=0, tiled=True
    )
    cells = local_frames * local_rows * local_cols
    windows = []
    grad_windows = []
    for tap_t in range(3):
        for tap_r in range(3):
            for tap_c in range(3):
                windows.append(
                    padded[
                        tap_t : tap_t + local_frames,
                        tap_r : tap_r + local_rows,
                        tap_c : tap_c + local_cols,
                    ]
                )
                grad_windows.append(
                    grad_ext[
                        2 - tap_t : 2 - tap_t + local_frames,
                        2 - tap_r : 2 - tap_r + local_rows,
                        2 - tap_c : 2 - tap_c + local_cols,
                    ]
                )
    patches = jnp.concatenate(windows, axis=-1).reshape(cells, 27 * channels)
    grad_patches = jnp.concatenate(grad_windows, axis=-1).reshape(cells, 27 * channels)
    conv = jnp.dot(patches, whole, preferred_element_type=jnp.float32) + conv_bias
    output = (video_f + conv.reshape(local_frames, local_rows, local_cols, channels)).astype(
        jnp.bfloat16
    )
    grad_flat = cotangent.reshape(cells, channels)
    kernel_grad = lax.dot_general(
        patches, grad_flat, (((0,), (0,)), ((), ())), preferred_element_type=jnp.float32
    )
    flipped = (
        whole.reshape(27, channels, channels).transpose(0, 2, 1).reshape(27 * channels, channels)
    )
    grad_hidden = jnp.dot(grad_patches, flipped, preferred_element_type=jnp.float32).astype(
        jnp.bfloat16
    )
    grad_hidden = lax.optimization_barrier(grad_hidden).astype(jnp.float32)
    grad_hidden = grad_hidden.reshape(local_frames, local_rows, local_cols, channels)
    normed = normed_ext[2:, 1:-1, 1:-1]
    pre = pre_ext[2:, 1:-1, 1:-1]
    sigma = jax.nn.sigmoid(pre)
    grad_pre = grad_hidden * sigma * (1.0 + pre * (1.0 - sigma))
    grad_f = cotangent.astype(jnp.float32)
    gain_part = jnp.sum(grad_pre * normed, axis=(0, 1, 2))
    shift_part = jnp.sum(grad_pre, axis=(0, 1, 2))
    bias_part = jnp.sum(grad_f, axis=(0, 1, 2))
    grad_gain, grad_shift, grad_conv_bias = all_sum(jnp.stack([gain_part, shift_part, bias_part]))
    row_count = lax.axis_size("rows")
    col_count = lax.axis_size("cols")
    band = kernel_grad.reshape(row_count, col_count, -1, channels)
    band = halve_scatter(band, "cols", 1)
    band = six_scatter(band.reshape(row_count, -1, channels), "rows")
    grad_weight = xor_sum(band, "tm")
    term_a = per_group(gain * grad_shift) / count
    term_b = per_group(gain * grad_gain) / count
    grad_video = (grad_f + rstd_c * (grad_pre * gain - term_a - normed * term_b)).astype(
        jnp.bfloat16
    )
    return (output, grad_video, grad_weight, grad_gain, grad_shift, grad_conv_bias)


def solution(mesh):
    return jax.shard_map(
        per_device,
        mesh=mesh,
        in_specs=(
            P("tm", "rows", "cols", None),
            P("tm", "rows", "cols", None),
            P(("rows", "cols"), None),
            P(),
            P(),
            P(),
        ),
        out_specs=(
            P("tm", "rows", "cols", None),
            P("tm", "rows", "cols", None),
            P(("rows", "cols"), None),
            P(),
            P(),
            P(),
        ),
        check_vma=False,
    )
```
